128 devices in a mesh: row: 8 (over x, y_lo), col: 16 (over y_hi, z, core).
Axes of the slice: x: 4, y: 4 (y_hi: 2, y_lo: 2; y = y_hi * 2 + y_lo), z: 4, core: 2. Of those that a mesh axis runs over, the one named last changes fastest.
Arguments:
- eigvecs: float32 [2048, 131072], P('col', 'row'), may hold values from -6 to 6
- basis: float32 [2, 131072, 256], P(None, 'row', 'col'), may hold values from -0.0625 to 0.0625
- coupling: float32 [2, 256, 256], replicated, as said below
Outputs:
- updated: float32 [2048, 131072], P(('col', 'row'))
The draws below stay inside these ranges and needn't reach their ends.
Inputs may be any that keep to these rules, and one draw needn't show every extreme that they name: `coupling`: each of the two matrices is upper triangular with a diagonal between 0.5 and 2.
All inputs are finite; a program needn't handle non-finite values.
Results may differ from the reference program's by a relative error of at most 0.00016.
Values sent between devices are 32-bit elements; how exact they have to be, the bound alone decides.
No kernel may reach another device: no remote copies, remote signals or barrier semaphores. Data moves between devices by JAX's collectives and lax.ppermute only.
A program may use at most 128 MiB of HBM per device.

```python
import math
import jax
import jax.numpy as jnp
from jax import lax

K = 256
NCOL = 2048
M = 131072


def draw_coupling(key, part):
    key_off = jax.random.fold_in(key, 11)
    key_diag = jax.random.fold_in(key, 23)
    offdiag = jax.random.normal(key_off, (2, K, K), jnp.float32)
    offdiag = offdiag * (1.0 / math.sqrt(K))
    diagonal = jnp.exp(jax.random.uniform(key_diag, (2, K), jnp.float32, math.log(0.5), math.log(2.0)))
    return jnp.triu(offdiag, 1) + diagonal[:, :, None] * jnp.eye(K, dtype=jnp.float32)[None, :, :]


def shard_levels(stream_key, dims, pieces, least, high):
    factor_of, own = 1.0, jax.random.fold_in(stream_key, 6)
    for axis_at, blocks in pieces:
        steps = jnp.exp(jax.random.uniform(jax.random.fold_in(own, axis_at), (blocks,), jnp.float32, least / len(pieces), high / len(pieces)))
        factor_of = factor_of * jnp.repeat(steps, dims[axis_at] // blocks).reshape([-1 if axis == axis_at else 1 for axis in range(len(dims))])
    return factor_of


def centred(key, extent, spread, most, split=(), held_as=jnp.bfloat16):
    values = jax.random.normal(key, extent, jnp.float32) * spread
    if len(split) > 0:
        values = shard_levels(key, extent, split, -0.22, 0.18) * values
    return jnp.clip(values, min=-most, max=most).astype(held_as)


def setup_inputs(seed: int = 0) -> dict:
    seeds = jax.random.split(jax.random.key(seed), 4)
    return {
        "eigvecs": centred(seeds[0], (NCOL, M), 1.0, 6.0, ((0, 16), (1, 8)), jnp.float32),
        "basis": centred(seeds[1], (2, M, K), (M // 16) ** -0.5, 0.0625, ((1, 8), (2, 16)), jnp.float32),
        "coupling": draw_coupling(jax.random.fold_in(seeds[3], 71), 0),
    }


def full_product(former, latter, contract_dims):
    return lax.dot_general(former, latter, (contract_dims, ((), ())), precision=lax.Precision.HIGHEST, preferred_element_type=jnp.float32)


def reference(eigvecs, basis, coupling):
    current = eigvecs
    for index_block in (1, 0):
        vectors = basis[index_block]
        projection = full_product(current, vectors, ((1,), (0,)))
        reflected = full_product(projection, coupling[index_block], ((1,), (1,)))
        current = current - full_product(reflected, vectors, ((1,), (1,)))
    return current
```

```python
import jax
import jax.numpy as jnp
from jax import lax
from jax.sharding import PartitionSpec as P


def full_product(former, latter, contract_dims):
    return lax.dot_general(
        former,
        latter,
        (contract_dims, ((), ())),
        precision=lax.Precision.HIGHEST,
        preferred_element_type=jnp.float32,
    )


def body(eigvecs, basis, coupling):
    panels = lax.all_gather(basis, "col", axis=2, tiled=True)
    inner_vectors = panels[1]
    outer_vectors = panels[0]
    k = inner_vectors.shape[1]
    proj_inner = full_product(eigvecs, inner_vectors, ((1,), (0,)))
    proj_outer = full_product(eigvecs, outer_vectors, ((1,), (0,)))
    gram = full_product(inner_vectors, outer_vectors, ((0,), (0,)))
    stacked = lax.psum(jnp.concatenate([proj_inner, proj_outer, gram], axis=0), "row")
    n = proj_inner.shape[0]
    proj_inner = stacked[:n]
    proj_outer = stacked[n:2 * n]
    gram = stacked[2 * n:2 * n + k]
    reflected_inner = full_product(proj_inner, coupling[1], ((1,), (1,)))
    proj_outer = proj_outer - full_product(reflected_inner, gram, ((1,), (0,)))
    reflected_outer = full_product(proj_outer, coupling[0], ((1,), (1,)))
    current = eigvecs - full_product(reflected_inner, inner_vectors, ((1,), (1,)))
    current = current - full_product(reflected_outer, outer_vectors, ((1,), (1,)))
    return lax.all_to_all(current, "row", split_axis=0, concat_axis=1, tiled=True)


def solution(mesh):
    placed = (P("col", "row"), P(None, "row", "col"), P())
    return jax.shard_map(
        body, mesh=mesh, in_specs=placed, out_specs=P(("col", "row"), None), check_vma=False
    )
```

```python
import jax
import jax.numpy as jnp
from jax import lax
from jax.sharding import PartitionSpec as P


def full_product(former, latter, contract_dims, precision=lax.Precision.HIGHEST):
    return lax.dot_general(
        former,
        latter,
        (contract_dims, ((), ())),
        precision=precision,
        preferred_element_type=jnp.float32,
    )


def large_product(former, latter, contract_dims):
    return full_product(former, latter, contract_dims, lax.Precision.HIGH)


def butterfly_sum(x, axis, size):
    step = 1
    while step < size:
        pairs = [(i, i ^ step) for i in range(size)]
        x = x + lax.ppermute(x, axis, pairs)
        step *= 2
    return x


def body(eigvecs, basis, coupling):
    panels = lax.all_gather(basis, "col", axis=2, tiled=True)
    inner_vectors = panels[1]
    outer_vectors = panels[0]
    k = inner_vectors.shape[1]
    proj_inner = large_product(eigvecs, inner_vectors, ((1,), (0,)))
    proj_outer = large_product(eigvecs, outer_vectors, ((1,), (0,)))
    gram = large_product(inner_vectors, outer_vectors, ((0,), (0,)))
    rows = lax.axis_size("row")
    stacked = butterfly_sum(jnp.concatenate([proj_inner, proj_outer, gram], axis=0), "row", rows)
    n = proj_inner.shape[0]
    proj_inner = stacked[:n]
    proj_outer = stacked[n:2 * n]
    gram = stacked[2 * n:2 * n + k]
    reflected_inner = full_product(proj_inner, coupling[1], ((1,), (1,)))
    proj_outer = proj_outer - full_product(reflected_inner, gram, ((1,), (0,)))
    reflected_outer = full_product(proj_outer, coupling[0], ((1,), (1,)))
    current = eigvecs - large_product(reflected_inner, inner_vectors, ((1,), (1,)))
    current = current - large_product(reflected_outer, outer_vectors, ((1,), (1,)))
    return lax.all_to_all(current, "row", split_axis=0, concat_axis=1, tiled=True)


def solution(mesh):
    placed = (P("col", "row"), P(None, "row", "col"), P())
    return jax.shard_map(
        body, mesh=mesh, in_specs=placed, out_specs=P(("col", "row"), None), check_vma=False
    )
```

```python
import jax
import jax.numpy as jnp
from jax import lax
from jax.sharding import PartitionSpec as P


def full_product(former, latter, contract_dims, precision=lax.Precision.HIGHEST):
    return lax.dot_general(
        former,
        latter,
        (contract_dims, ((), ())),
        precision=precision,
        preferred_element_type=jnp.float32,
    )


def large_product(former, latter, contract_dims):
    return full_product(former, latter, contract_dims, lax.Precision.HIGH)


def butterfly_sum(x, axis, size):
    step = 1
    while step < size:
        pairs = [(i, i ^ step) for i in range(size)]
        x = x + lax.ppermute(x, axis, pairs)
        step *= 2
    return x


def body(eigvecs, basis, coupling):
    local_rows = basis.shape[1]
    half = local_rows // 2
    pieces = ((0, half), (half, local_rows))
    panels = [
        lax.all_gather(basis[:, lo:hi, :], "col", axis=2, tiled=True) for lo, hi in pieces
    ]
    n = eigvecs.shape[0]
    k = panels[0].shape[2]
    proj = None
    gram = None
    for (lo, hi), panel in zip(pieces, panels):
        part = large_product(eigvecs[:, lo:hi], panel, ((1,), (1,)))
        g = large_product(panel[1], panel[0], ((0,), (0,)))
        proj = part if proj is None else proj + part
        gram = g if gram is None else gram + g
    rows = lax.axis_size("row")
    stacked = butterfly_sum(
        jnp.concatenate([proj[:, 1, :], proj[:, 0, :], gram], axis=0), "row", rows
    )
    proj_inner = stacked[:n]
    proj_outer = stacked[n:2 * n]
    gram = stacked[2 * n:2 * n + k]
    reflected_inner = full_product(proj_inner, coupling[1], ((1,), (1,)))
    proj_outer = proj_outer - full_product(reflected_inner, gram, ((1,), (0,)))
    reflected_outer = full_product(proj_outer, coupling[0], ((1,), (1,)))
    reflected = jnp.stack([reflected_outer, reflected_inner], axis=1)
    halves = [
        eigvecs[:, lo:hi] - large_product(reflected, panel, ((1, 2), (0, 2)))
        for (lo, hi), panel in zip(pieces, panels)
    ]
    current = jnp.concatenate(halves, axis=1)
    return lax.all_to_all(current, "row", split_axis=0, concat_axis=1, tiled=True)


def solution(mesh):
    placed = (P("col", "row"), P(None, "row", "col"), P())
    return jax.shard_map(
        body, mesh=mesh, in_specs=placed, out_specs=P(("col", "row"), None), check_vma=False
    )
```

```python
import jax
import jax.numpy as jnp
from jax import lax
from jax.sharding import PartitionSpec as P


def full_product(former, latter, contract_dims, precision=lax.Precision.HIGHEST):
    return lax.dot_general(
        former,
        latter,
        (contract_dims, ((), ())),
        precision=precision,
        preferred_element_type=jnp.float32,
    )


def large_product(former, latter, contract_dims):
    return full_product(former, latter, contract_dims, lax.Precision.HIGH)


def butterfly_sum(x, axis, size):
    step = 1
    while step < size:
        pairs = [(i, i ^ step) for i in range(size)]
        x = x + lax.ppermute(x, axis, pairs)
        step *= 2
    return x


def body(eigvecs, basis, coupling):
    panel = lax.all_gather(basis, "col", axis=2, tiled=True)
    n = eigvecs.shape[0]
    k = panel.shape[2]
    proj = large_product(eigvecs, panel, ((1,), (1,)))
    gram = large_product(panel[1], panel[0], ((0,), (0,)))
    rows = lax.axis_size("row")
    stacked = butterfly_sum(
        jnp.concatenate([proj[:, 1, :], proj[:, 0, :], gram], axis=0), "row", rows
    )
    proj_inner = stacked[:n]
    proj_outer = stacked[n:2 * n]
    gram = stacked[2 * n:2 * n + k]
    reflected_inner = full_product(proj_inner, coupling[1], ((1,), (1,)))
    proj_outer = proj_outer - full_product(reflected_inner, gram, ((1,), (0,)))
    reflected_outer = full_product(proj_outer, coupling[0], ((1,), (1,)))
    reflected = jnp.stack([reflected_outer, reflected_inner], axis=1)
    current = eigvecs - large_product(reflected, panel, ((1, 2), (0, 2)))
    return lax.all_to_all(current, "row", split_axis=0, concat_axis=1, tiled=True)


def solution(mesh):
    placed = (P("col", "row"), P(None, "row", "col"), P())
    return jax.shard_map(
        body, mesh=mesh, in_specs=placed, out_specs=P(("col", "row"), None), check_vma=False
    )
```

```python
import jax
import jax.numpy as jnp
from jax import lax
from jax.sharding import PartitionSpec as P


def full_product(former, latter, contract_dims, precision=lax.Precision.HIGHEST):
    return lax.dot_general(
        former,
        latter,
        (contract_dims, ((), ())),
        precision=precision,
        preferred_element_type=jnp.float32,
    )


def large_product(former, latter, contract_dims):
    return full_product(former, latter, contract_dims, lax.Precision.HIGH)


def butterfly_sum(x, axis, size):
    step = 1
    while step < size:
        pairs = [(i, i ^ step) for i in range(size)]
        x = x + lax.ppermute(x, axis, pairs)
        step *= 2
    return x


def body(eigvecs, basis, coupling):
    panel = lax.all_gather(basis, "col", axis=2, tiled=True)
    n = eigvecs.shape[0]
    k = panel.shape[2]
    proj = large_product(eigvecs, panel, ((1,), (1,)))
    gram = large_product(panel[1], panel[0], ((0,), (0,)))
    rows = lax.axis_size("row")
    stacked = butterfly_sum(
        jnp.concatenate([proj[:, 1, :], proj[:, 0, :], gram], axis=0), "row", rows
    )
    proj_inner = stacked[:n]
    proj_outer = stacked[n:2 * n]
    gram = stacked[2 * n:2 * n + k]
    reflected_inner = full_product(proj_inner, coupling[1], ((1,), (1,)))
    proj_outer = proj_outer - full_product(reflected_inner, gram, ((1,), (0,)))
    reflected_outer = full_product(proj_outer, coupling[0], ((1,), (1,)))
    reflected = jnp.stack([reflected_outer, reflected_inner], axis=1)
    me = lax.axis_index("row")
    block_rows = n // rows
    width = eigvecs.shape[1]
    half = width // 2
    updated = jnp.zeros((block_rows, rows * width), eigvecs.dtype)
    for lo in (0, half):
        current = eigvecs[:, lo:lo + half] - large_product(
            reflected, panel[:, lo:lo + half, :], ((1, 2), (0, 2))
        )
        for shift in range(rows):
            dest = (me + shift) % rows
            src = (me - shift) % rows
            block = lax.dynamic_slice_in_dim(current, dest * block_rows, block_rows, axis=0)
            if shift:
                block = lax.ppermute(block, "row", [(i, (i + shift) % rows) for i in range(rows)])
            updated = lax.dynamic_update_slice_in_dim(updated, block, src * width + lo, axis=1)
    return updated


def solution(mesh):
    placed = (P("col", "row"), P(None, "row", "col"), P())
    return jax.shard_map(
        body, mesh=mesh, in_specs=placed, out_specs=P(("col", "row"), None), check_vma=False
    )
```

```python
import jax
import jax.numpy as jnp
from jax import lax
import numpy as np
from jax.sharding import Mesh, PartitionSpec as P


def full_product(former, latter, contract_dims, precision=lax.Precision.HIGHEST):
    return lax.dot_general(
        former,
        latter,
        (contract_dims, ((), ())),
        precision=precision,
        preferred_element_type=jnp.float32,
    )


def large_product(former, latter, contract_dims):
    return full_product(former, latter, contract_dims, lax.Precision.HIGH)


def butterfly_sum(x, axis, size):
    step = 1
    while step < size:
        pairs = [(i, i ^ step) for i in range(size)]
        x = x + lax.ppermute(x, axis, pairs)
        step *= 2
    return x


def body(eigvecs, basis, coupling):
    upper = lax.axis_index("yhi") == 1
    partner = lax.ppermute(basis, "yhi", [(0, 1), (1, 0)])
    lower_piece = jnp.where(upper, partner, basis)
    upper_piece = jnp.where(upper, basis, partner)
    panel = lax.all_gather(
        jnp.concatenate([lower_piece, upper_piece], axis=2), "zc", axis=2, tiled=True
    )
    halves = lax.axis_size("yhi")
    groups = lax.axis_size("zc")
    piece = basis.shape[2]
    order = np.arange(halves * groups * piece).reshape(halves, groups, piece).transpose(1, 0, 2).reshape(-1)
    coupling = coupling[:, order][:, :, order]
    n = eigvecs.shape[0]
    k = panel.shape[2]
    proj = large_product(eigvecs, panel, ((1,), (1,)))
    gram = large_product(panel[1], panel[0], ((0,), (0,)))
    rows = lax.axis_size("row")
    stacked = butterfly_sum(
        jnp.concatenate([proj[:, 1, :], proj[:, 0, :], gram], axis=0), "row", rows
    )
    proj_inner = stacked[:n]
    proj_outer = stacked[n:2 * n]
    gram = stacked[2 * n:2 * n + k]
    reflected_inner = full_product(proj_inner, coupling[1], ((1,), (1,)))
    proj_outer = proj_outer - full_product(reflected_inner, gram, ((1,), (0,)))
    reflected_outer = full_product(proj_outer, coupling[0], ((1,), (1,)))
    reflected = jnp.stack([reflected_outer, reflected_inner], axis=1)
    current = eigvecs - large_product(reflected, panel, ((1, 2), (0, 2)))
    return lax.all_to_all(current, "row", split_axis=0, concat_axis=1, tiled=True)


def solution(mesh):
    rows, cols = mesh.devices.shape
    split = Mesh(mesh.devices.reshape(rows, 2, cols // 2), ("row", "yhi", "zc"))
    col = ("yhi", "zc")
    placed = (P(col, "row"), P(None, "row", col), P())
    return jax.shard_map(
        body, mesh=split, in_specs=placed, out_specs=P(("yhi", "zc", "row"), None), check_vma=False
    )
```

```python
import jax
import jax.numpy as jnp
from jax import lax
from jax.experimental import pallas as pl
from jax.experimental.pallas import tpu as pltpu
from jax.sharding import PartitionSpec as P


def full_product(former, latter, contract_dims, precision=lax.Precision.HIGHEST):
    return lax.dot_general(
        former,
        latter,
        (contract_dims, ((), ())),
        precision=precision,
        preferred_element_type=jnp.float32,
    )


def large_product(former, latter, contract_dims):
    return full_product(former, latter, contract_dims, lax.Precision.HIGH)


def butterfly_sum(x, axis, size):
    step = 1
    while step < size:
        pairs = [(i, i ^ step) for i in range(size)]
        x = x + lax.ppermute(x, axis, pairs)
        step *= 2
    return x


def _split(x):
    hi = x.astype(jnp.bfloat16)
    lo = (x - hi.astype(jnp.float32)).astype(jnp.bfloat16)
    return hi, lo

def _dot_nt(a, b):
    return lax.dot_general(a, b, (((1,), (1,)), ((), ())), preferred_element_type=jnp.float32)

def _dot3(a, b):
    return _dot_nt(a[0], b[0]) + _dot_nt(a[0], b[1]) + _dot_nt(a[1], b[0])

def _proj_kernel(e_ref, v_ref, proj_ref, gram_ref):
    @pl.when(pl.program_id(0) == 0)
    def _():
        proj_ref[...] = jnp.zeros_like(proj_ref)
        gram_ref[...] = jnp.zeros_like(gram_ref)
    e = _split(e_ref[...])
    outer = _split(v_ref[0])
    inner = _split(v_ref[1])
    proj_ref[0] += _dot3(e, outer)
    proj_ref[1] += _dot3(e, inner)
    gram_ref[...] += _dot3(inner, outer)

def project(eigvecs, panel_t, tile):
    n, m = eigvecs.shape
    k = panel_t.shape[1]
    return pl.pallas_call(
        _proj_kernel,
        grid=(m // tile,),
        in_specs=[pl.BlockSpec((n, tile), lambda i: (0, i)),
                  pl.BlockSpec((2, k, tile), lambda i: (0, 0, i))],
        out_specs=[pl.BlockSpec((2, n, k), lambda i: (0, 0, 0)),
                   pl.BlockSpec((k, k), lambda i: (0, 0))],
        out_shape=[jax.ShapeDtypeStruct((2, n, k), jnp.float32),
                   jax.ShapeDtypeStruct((k, k), jnp.float32)],
        compiler_params=pltpu.CompilerParams(dimension_semantics=("arbitrary",)),
    )(eigvecs, panel_t)


def body(eigvecs, basis, coupling):
    panel = lax.all_gather(jnp.swapaxes(basis, 1, 2), "col", axis=1, tiled=True)
    n = eigvecs.shape[0]
    k = panel.shape[1]
    proj, gram = project(eigvecs, panel, 2048)
    rows = lax.axis_size("row")
    stacked = butterfly_sum(
        jnp.concatenate([proj[1], proj[0], gram], axis=0), "row", rows
    )
    proj_inner = stacked[:n]
    proj_outer = stacked[n:2 * n]
    gram = stacked[2 * n:2 * n + k]
    reflected_inner = full_product(proj_inner, coupling[1], ((1,), (1,)))
    proj_outer = proj_outer - full_product(reflected_inner, gram, ((1,), (0,)))
    reflected_outer = full_product(proj_outer, coupling[0], ((1,), (1,)))
    reflected = jnp.stack([reflected_outer, reflected_inner], axis=1)
    current = eigvecs - large_product(reflected, panel, ((1, 2), (0, 1)))
    return lax.all_to_all(current, "row", split_axis=0, concat_axis=1, tiled=True)


def solution(mesh):
    placed = (P("col", "row"), P(None, "row", "col"), P())
    return jax.shard_map(
        body, mesh=mesh, in_specs=placed, out_specs=P(("col", "row"), None), check_vma=False
    )
```

```python
import jax
import jax.numpy as jnp
from jax import lax
from jax.experimental import pallas as pl
from jax.experimental.pallas import tpu as pltpu
from jax.sharding import PartitionSpec as P


def full_product(former, latter, contract_dims, precision=lax.Precision.HIGHEST):
    return lax.dot_general(
        former,
        latter,
        (contract_dims, ((), ())),
        precision=precision,
        preferred_element_type=jnp.float32,
    )


def large_product(former, latter, contract_dims):
    return full_product(former, latter, contract_dims, lax.Precision.HIGH)


def butterfly_sum(x, axis, size):
    step = 1
    while step < size:
        pairs = [(i, i ^ step) for i in range(size)]
        x = x + lax.ppermute(x, axis, pairs)
        step *= 2
    return x


def _split(x):
    hi = x.astype(jnp.bfloat16)
    lo = (x - hi.astype(jnp.float32)).astype(jnp.bfloat16)
    return hi, lo

def _dot_nt(a, b):
    return lax.dot_general(a, b, (((1,), (1,)), ((), ())), preferred_element_type=jnp.float32)

def _dot3(a, b):
    return _dot_nt(a[0], b[0]) + _dot_nt(a[0], b[1]) + _dot_nt(a[1], b[0])

def _proj_kernel(e_hi_ref, e_lo_ref, v_ref, out_ref):
    @pl.when(pl.program_id(0) == 0)
    def _():
        out_ref[...] = jnp.zeros_like(out_ref)
    n = e_hi_ref.shape[0]
    k = v_ref.shape[1]
    e = (e_hi_ref[...], e_lo_ref[...])
    outer = _split(v_ref[0])
    inner = _split(v_ref[1])
    out_ref[0:n] += _dot3(e, inner)
    out_ref[n:2 * n] += _dot3(e, outer)
    out_ref[2 * n:2 * n + k] += _dot3(inner, outer)


def project(eigvecs, panel_t, tile):
    n, m = eigvecs.shape
    k = panel_t.shape[1]
    high = lax.reduce_precision(eigvecs, exponent_bits=8, mantissa_bits=7)
    e_hi = high.astype(jnp.bfloat16)
    e_lo = (eigvecs - high).astype(jnp.bfloat16)
    return pl.pallas_call(
        _proj_kernel,
        grid=(m // tile,),
        in_specs=[pl.BlockSpec((n, tile), lambda i: (0, i)),
                  pl.BlockSpec((n, tile), lambda i: (0, i)),
                  pl.BlockSpec((2, k, tile), lambda i: (0, 0, i))],
        out_specs=pl.BlockSpec((2 * n + k, k), lambda i: (0, 0)),
        out_shape=jax.ShapeDtypeStruct((2 * n + k, k), jnp.float32),
        compiler_params=pltpu.CompilerParams(dimension_semantics=("arbitrary",)),
    )(e_hi, e_lo, panel_t)


def body(eigvecs, basis, coupling):
    panel = lax.all_gather(jnp.swapaxes(basis, 1, 2), "col", axis=1, tiled=True)
    n = eigvecs.shape[0]
    k = panel.shape[1]
    rows = lax.axis_size("row")
    stacked = butterfly_sum(project(eigvecs, panel, 2048), "row", rows)
    proj_inner = stacked[:n]
    proj_outer = stacked[n:2 * n]
    gram = stacked[2 * n:2 * n + k]
    reflected_inner = full_product(proj_inner, coupling[1], ((1,), (1,)))
    proj_outer = proj_outer - full_product(reflected_inner, gram, ((1,), (0,)))
    reflected_outer = full_product(proj_outer, coupling[0], ((1,), (1,)))
    reflected = jnp.stack([reflected_outer, reflected_inner], axis=1)
    current = eigvecs - large_product(reflected, panel, ((1, 2), (0, 1)))
    return lax.all_to_all(current, "row", split_axis=0, concat_axis=1, tiled=True)


def solution(mesh):
    placed = (P("col", "row"), P(None, "row", "col"), P())
    return jax.shard_map(
        body, mesh=mesh, in_specs=placed, out_specs=P(("col", "row"), None), check_vma=False
    )
```

```python
import jax
import jax.numpy as jnp
from jax import lax
from jax.experimental import pallas as pl
from jax.experimental.pallas import tpu as pltpu
from jax.sharding import PartitionSpec as P


def full_product(former, latter, contract_dims, precision=lax.Precision.HIGHEST):
    return lax.dot_general(
        former,
        latter,
        (contract_dims, ((), ())),
        precision=precision,
        preferred_element_type=jnp.float32,
    )


def large_product(former, latter, contract_dims):
    return full_product(former, latter, contract_dims, lax.Precision.HIGH)


def butterfly_sum(x, axis, size):
    step = 1
    while step < size:
        pairs = [(i, i ^ step) for i in range(size)]
        x = x + lax.ppermute(x, axis, pairs)
        step *= 2
    return x


def _split(x):
    hi = x.astype(jnp.bfloat16)
    lo = (x - hi.astype(jnp.float32)).astype(jnp.bfloat16)
    return hi, lo

def _dot_nt(a, b):
    return lax.dot_general(a, b, (((1,), (1,)), ((), ())), preferred_element_type=jnp.float32)

def _dot3(a, b):
    return _dot_nt(a[0], b[0]) + _dot_nt(a[0], b[1]) + _dot_nt(a[1], b[0])

def _proj_kernel(e_hi_ref, e_lo_ref, v_ref, out_ref):
    @pl.when(pl.program_id(0) == 0)
    def _():
        out_ref[...] = jnp.zeros_like(out_ref)
    n = e_hi_ref.shape[0]
    k = v_ref.shape[1]
    e = (e_hi_ref[...], e_lo_ref[...])
    outer = _split(v_ref[0])
    inner = _split(v_ref[1])
    out_ref[0:n] += _dot3(e, inner)
    out_ref[n:2 * n] += _dot3(e, outer)
    out_ref[2 * n:2 * n + k] += _dot3(inner, outer)


def project(eigvecs, panel_t, tile):
    n, m = eigvecs.shape
    k = panel_t.shape[1]
    high = lax.reduce_precision(eigvecs, exponent_bits=8, mantissa_bits=7)
    e_hi = high.astype(jnp.bfloat16)
    e_lo = (eigvecs - high).astype(jnp.bfloat16)
    return pl.pallas_call(
        _proj_kernel,
        grid=(m // tile,),
        in_specs=[pl.BlockSpec((n, tile), lambda i: (0, i)),
                  pl.BlockSpec((n, tile), lambda i: (0, i)),
                  pl.BlockSpec((2, k, tile), lambda i: (0, 0, i))],
        out_specs=pl.BlockSpec((2 * n + k, k), lambda i: (0, 0)),
        out_shape=jax.ShapeDtypeStruct((2 * n + k, k), jnp.float32),
        compiler_params=pltpu.CompilerParams(dimension_semantics=("arbitrary",)),
    )(e_hi, e_lo, panel_t)


def body(eigvecs, basis, coupling):
    panel = lax.all_gather(jnp.swapaxes(basis, 1, 2), "col", axis=1, tiled=True)
    n = eigvecs.shape[0]
    k = panel.shape[1]
    rows = lax.axis_size("row")
    partial = project(eigvecs, panel, 2048)
    stacked = jnp.concatenate(
        [butterfly_sum(partial[:2 * n], "row", rows), butterfly_sum(partial[2 * n:], "row", rows)],
        axis=0,
    )
    proj_inner = stacked[:n]
    proj_outer = stacked[n:2 * n]
    gram = stacked[2 * n:2 * n + k]
    reflected_inner = full_product(proj_inner, coupling[1], ((1,), (1,)))
    proj_outer = proj_outer - full_product(reflected_inner, gram, ((1,), (0,)))
    reflected_outer = full_product(proj_outer, coupling[0], ((1,), (1,)))
    reflected = jnp.stack([reflected_outer, reflected_inner], axis=1)
    current = eigvecs - large_product(reflected, panel, ((1, 2), (0, 1)))
    return lax.all_to_all(current, "row", split_axis=0, concat_axis=1, tiled=True)


def solution(mesh):
    placed = (P("col", "row"), P(None, "row", "col"), P())
    return jax.shard_map(
        body, mesh=mesh, in_specs=placed, out_specs=P(("col", "row"), None), check_vma=False
    )
```

```python
import jax
import jax.numpy as jnp
from jax import lax
from jax.experimental import pallas as pl
from jax.experimental.pallas import tpu as pltpu
from jax.sharding import PartitionSpec as P


def full_product(former, latter, contract_dims, precision=lax.Precision.HIGHEST):
    return lax.dot_general(
        former,
        latter,
        (contract_dims, ((), ())),
        precision=precision,
        preferred_element_type=jnp.float32,
    )


def large_product(former, latter, contract_dims):
    return full_product(former, latter, contract_dims, lax.Precision.HIGH)


def butterfly_sum(x, axis, size):
    step = 1
    while step < size:
        pairs = [(i, i ^ step) for i in range(size)]
        x = jax.tree_util.tree_map(jnp.add, x, lax.ppermute(x, axis, pairs))
        step *= 2
    return x


def _split(x):
    hi = x.astype(jnp.bfloat16)
    lo = (x - hi.astype(jnp.float32)).astype(jnp.bfloat16)
    return hi, lo

def _dot_nt(a, b):
    return lax.dot_general(a, b, (((1,), (1,)), ((), ())), preferred_element_type=jnp.float32)

def _dot3(a, b):
    return _dot_nt(a[0], b[0]) + _dot_nt(a[0], b[1]) + _dot_nt(a[1], b[0])

def _dot_nn(a, b):
    return lax.dot_general(a, b, (((1,), (0,)), ((), ())), preferred_element_type=jnp.float32)


def _proj_kernel(et_hi_ref, et_lo_ref, v_ref, pt_ref, gram_ref):
    @pl.when(pl.program_id(0) == 0)
    def _():
        pt_ref[...] = jnp.zeros_like(pt_ref)
        gram_ref[...] = jnp.zeros_like(gram_ref)
    et = (et_hi_ref[...], et_lo_ref[...])
    outer = _split(v_ref[0])
    inner = _split(v_ref[1])
    pt_ref[0] += _dot_nn(outer[0], et[0]) + _dot_nn(outer[0], et[1]) + _dot_nn(outer[1], et[0])
    pt_ref[1] += _dot_nn(inner[0], et[0]) + _dot_nn(inner[0], et[1]) + _dot_nn(inner[1], et[0])
    gram_ref[...] += _dot3(inner, outer)


def project(eigvecs, panel_t, tile):
    n, m = eigvecs.shape
    k = panel_t.shape[1]
    high = lax.reduce_precision(eigvecs, exponent_bits=8, mantissa_bits=7)
    et_hi = high.T.astype(jnp.bfloat16)
    et_lo = (eigvecs - high).T.astype(jnp.bfloat16)
    return pl.pallas_call(
        _proj_kernel,
        grid=(m // tile,),
        in_specs=[pl.BlockSpec((tile, n), lambda i: (i, 0)),
                  pl.BlockSpec((tile, n), lambda i: (i, 0)),
                  pl.BlockSpec((2, k, tile), lambda i: (0, 0, i))],
        out_specs=[pl.BlockSpec((2, k, n), lambda i: (0, 0, 0)),
                   pl.BlockSpec((k, k), lambda i: (0, 0))],
        out_shape=[jax.ShapeDtypeStruct((2, k, n), jnp.float32),
                   jax.ShapeDtypeStruct((k, k), jnp.float32)],
        compiler_params=pltpu.CompilerParams(dimension_semantics=("arbitrary",)),
    )(et_hi, et_lo, panel_t)


def body(eigvecs, basis, coupling):
    panel = lax.all_gather(jnp.swapaxes(basis, 1, 2), "col", axis=1, tiled=True)
    n = eigvecs.shape[0]
    k = panel.shape[1]
    rows = lax.axis_size("row")
    proj_t, gram = butterfly_sum(project(eigvecs, panel, 2048), "row", rows)
    proj_inner = proj_t[1].T
    proj_outer = proj_t[0].T
    reflected_inner = full_product(proj_inner, coupling[1], ((1,), (1,)))
    proj_outer = proj_outer - full_product(reflected_inner, gram, ((1,), (0,)))
    reflected_outer = full_product(proj_outer, coupling[0], ((1,), (1,)))
    reflected = jnp.stack([reflected_outer, reflected_inner], axis=1)
    current = eigvecs - large_product(reflected, panel, ((1, 2), (0, 1)))
    return lax.all_to_all(current, "row", split_axis=0, concat_axis=1, tiled=True)


def solution(mesh):
    placed = (P("col", "row"), P(None, "row", "col"), P())
    return jax.shard_map(
        body, mesh=mesh, in_specs=placed, out_specs=P(("col", "row"), None), check_vma=False
    )
```

```python
import jax
import jax.numpy as jnp
from jax import lax
from jax.experimental import pallas as pl
from jax.experimental.pallas import tpu as pltpu
from jax.sharding import PartitionSpec as P


def full_product(former, latter, contract_dims, precision=lax.Precision.HIGHEST):
    return lax.dot_general(
        former,
        latter,
        (contract_dims, ((), ())),
        precision=precision,
        preferred_element_type=jnp.float32,
    )


def large_product(former, latter, contract_dims):
    return full_product(former, latter, contract_dims, lax.Precision.HIGH)


def butterfly_sum(x, axis, size):
    step = 1
    while step < size:
        pairs = [(i, i ^ step) for i in range(size)]
        x = jax.tree_util.tree_map(jnp.add, x, lax.ppermute(x, axis, pairs))
        step *= 2
    return x


def _split(x):
    hi = x.astype(jnp.bfloat16)
    lo = (x - hi.astype(jnp.float32)).astype(jnp.bfloat16)
    return hi, lo

def _dot_nt(a, b):
    return lax.dot_general(a, b, (((1,), (1,)), ((), ())), preferred_element_type=jnp.float32)

def _dot3(a, b):
    return _dot_nt(a[0], b[0]) + _dot_nt(a[0], b[1]) + _dot_nt(a[1], b[0])

def _dot_nn(a, b):
    return lax.dot_general(a, b, (((1,), (0,)), ((), ())), preferred_element_type=jnp.float32)


def _proj_kernel(et_hi_ref, et_lo_ref, v_ref, outer_ref, inner_ref, gram_lo_ref, gram_hi_ref):
    outs = (outer_ref, inner_ref, gram_lo_ref, gram_hi_ref)

    @pl.when(pl.program_id(0) == 0)
    def _():
        for ref in outs:
            ref[...] = jnp.zeros_like(ref)
    et = (et_hi_ref[...], et_lo_ref[...])
    outer = _split(v_ref[0])
    inner = _split(v_ref[1])
    outer_ref[...] += _dot_nn(outer[0], et[0]) + _dot_nn(outer[0], et[1]) + _dot_nn(outer[1], et[0])
    inner_ref[...] += _dot_nn(inner[0], et[0]) + _dot_nn(inner[0], et[1]) + _dot_nn(inner[1], et[0])
    half = gram_lo_ref.shape[0]
    gram_lo_ref[...] += _dot3((inner[0][:half], inner[1][:half]), outer)
    gram_hi_ref[...] += _dot3((inner[0][half:], inner[1][half:]), outer)


def project(eigvecs, panel_t, tile):
    n, m = eigvecs.shape
    k = panel_t.shape[1]
    high = lax.reduce_precision(eigvecs, exponent_bits=8, mantissa_bits=7)
    et_hi = high.T.astype(jnp.bfloat16)
    et_lo = (eigvecs - high).T.astype(jnp.bfloat16)
    return pl.pallas_call(
        _proj_kernel,
        grid=(m // tile,),
        in_specs=[pl.BlockSpec((tile, n), lambda i: (i, 0)),
                  pl.BlockSpec((tile, n), lambda i: (i, 0)),
                  pl.BlockSpec((2, k, tile), lambda i: (0, 0, i))],
        out_specs=[pl.BlockSpec((k, n), lambda i: (0, 0))] * 2
        + [pl.BlockSpec((k // 2, k), lambda i: (0, 0))] * 2,
        out_shape=[jax.ShapeDtypeStruct((k, n), jnp.float32)] * 2
        + [jax.ShapeDtypeStruct((k // 2, k), jnp.float32)] * 2,
        compiler_params=pltpu.CompilerParams(dimension_semantics=("arbitrary",)),
    )(et_hi, et_lo, panel_t)


def body(eigvecs, basis, coupling):
    panel = lax.all_gather(jnp.swapaxes(basis, 1, 2), "col", axis=1, tiled=True)
    n = eigvecs.shape[0]
    k = panel.shape[1]
    rows = lax.axis_size("row")
    outer_t, inner_t, gram_lo, gram_hi = butterfly_sum(project(eigvecs, panel, 2048), "row", rows)
    gram = jnp.concatenate([gram_lo, gram_hi], axis=0)
    proj_inner = inner_t.T
    proj_outer = outer_t.T
    reflected_inner = full_product(proj_inner, coupling[1], ((1,), (1,)))
    proj_outer = proj_outer - full_product(reflected_inner, gram, ((1,), (0,)))
    reflected_outer = full_product(proj_outer, coupling[0], ((1,), (1,)))
    reflected = jnp.stack([reflected_outer, reflected_inner], axis=1)
    current = eigvecs - large_product(reflected, panel, ((1, 2), (0, 1)))
    return lax.all_to_all(current, "row", split_axis=0, concat_axis=1, tiled=True)


def solution(mesh):
    placed = (P("col", "row"), P(None, "row", "col"), P())
    return jax.shard_map(
        body, mesh=mesh, in_specs=placed, out_specs=P(("col", "row"), None), check_vma=False
    )
```

```python
import jax
import jax.numpy as jnp
from jax import lax
from jax.experimental import pallas as pl
from jax.experimental.pallas import tpu as pltpu
from jax.sharding import PartitionSpec as P


def full_product(former, latter, contract_dims, precision=lax.Precision.HIGHEST):
    return lax.dot_general(
        former,
        latter,
        (contract_dims, ((), ())),
        precision=precision,
        preferred_element_type=jnp.float32,
    )


def large_product(former, latter, contract_dims):
    return full_product(former, latter, contract_dims, lax.Precision.HIGH)


def butterfly_sum(x, axis, size):
    step = 1
    while step < size:
        pairs = [(i, i ^ step) for i in range(size)]
        x = jax.tree_util.tree_map(jnp.add, x, lax.ppermute(x, axis, pairs))
        step *= 2
    return x


def _split(x):
    hi = x.astype(jnp.bfloat16)
    lo = (x - hi.astype(jnp.float32)).astype(jnp.bfloat16)
    return hi, lo

def _dot_nt(a, b):
    return lax.dot_general(a, b, (((1,), (1,)), ((), ())), preferred_element_type=jnp.float32)

def _dot3(a, b):
    return _dot_nt(a[0], b[0]) + _dot_nt(a[0], b[1]) + _dot_nt(a[1], b[0])

def _dot_nn(a, b):
    return lax.dot_general(a, b, (((1,), (0,)), ((), ())), preferred_element_type=jnp.float32)


def _proj_kernel(et_hi_ref, et_lo_ref, v_ref, outer_ref, inner_ref, gram_ref):
    @pl.when(pl.program_id(0) == 0)
    def _():
        outer_ref[...] = jnp.zeros_like(outer_ref)
        inner_ref[...] = jnp.zeros_like(inner_ref)
        gram_ref[...] = jnp.zeros_like(gram_ref)
    et = (et_hi_ref[...], et_lo_ref[...])
    outer = _split(v_ref[0])
    inner = _split(v_ref[1])
    outer_ref[...] += _dot_nn(outer[0], et[0]) + _dot_nn(outer[0], et[1]) + _dot_nn(outer[1], et[0])
    inner_ref[...] += _dot_nn(inner[0], et[0]) + _dot_nn(inner[0], et[1]) + _dot_nn(inner[1], et[0])
    gram_ref[...] += _dot3(inner, outer)


def project(eigvecs, panel_t, tile):
    n, m = eigvecs.shape
    k = panel_t.shape[1]
    high = lax.reduce_precision(eigvecs, exponent_bits=8, mantissa_bits=7)
    et_hi = high.T.astype(jnp.bfloat16)
    et_lo = (eigvecs - high).T.astype(jnp.bfloat16)
    return pl.pallas_call(
        _proj_kernel,
        grid=(m // tile,),
        in_specs=[pl.BlockSpec((tile, n), lambda i: (i, 0)),
                  pl.BlockSpec((tile, n), lambda i: (i, 0)),
                  pl.BlockSpec((2, k, tile), lambda i: (0, 0, i))],
        out_specs=[pl.BlockSpec((k, n), lambda i: (0, 0)),
                   pl.BlockSpec((k, n), lambda i: (0, 0)),
                   pl.BlockSpec((k, k), lambda i: (0, 0))],
        out_shape=[jax.ShapeDtypeStruct((k, n), jnp.float32),
                   jax.ShapeDtypeStruct((k, n), jnp.float32),
                   jax.ShapeDtypeStruct((k, k), jnp.float32)],
        compiler_params=pltpu.CompilerParams(dimension_semantics=("arbitrary",)),
    )(et_hi, et_lo, panel_t)


def body(eigvecs, basis, coupling):
    panel = lax.all_gather(jnp.swapaxes(basis, 1, 2), "col", axis=1, tiled=True)
    n = eigvecs.shape[0]
    k = panel.shape[1]
    rows = lax.axis_size("row")
    outer_t, inner_t, gram = butterfly_sum(project(eigvecs, panel, 2048), "row", rows)
    proj_inner = inner_t.T
    proj_outer = outer_t.T
    reflected_inner = full_product(proj_inner, coupling[1], ((1,), (1,)))
    proj_outer = proj_outer - full_product(reflected_inner, gram, ((1,), (0,)))
    reflected_outer = full_product(proj_outer, coupling[0], ((1,), (1,)))
    reflected = jnp.stack([reflected_outer, reflected_inner], axis=1)
    current = eigvecs - large_product(reflected, panel, ((1, 2), (0, 1)))
    return lax.all_to_all(current, "row", split_axis=0, concat_axis=1, tiled=True)


def solution(mesh):
    placed = (P("col", "row"), P(None, "row", "col"), P())
    return jax.shard_map(
        body, mesh=mesh, in_specs=placed, out_specs=P(("col", "row"), None), check_vma=False
    )
```

```python
import jax
import jax.numpy as jnp
from jax import lax
from jax.experimental import pallas as pl
from jax.experimental.pallas import tpu as pltpu
from jax.sharding import PartitionSpec as P


def full_product(former, latter, contract_dims, precision=lax.Precision.HIGHEST):
    return lax.dot_general(
        former,
        latter,
        (contract_dims, ((), ())),
        precision=precision,
        preferred_element_type=jnp.float32,
    )


def large_product(former, latter, contract_dims):
    return full_product(former, latter, contract_dims, lax.Precision.HIGH)


def butterfly_sum(x, axis, size):
    step = 1
    while step < size:
        pairs = [(i, i ^ step) for i in range(size)]
        x = jax.tree_util.tree_map(jnp.add, x, lax.ppermute(x, axis, pairs))
        step *= 2
    return x


def _split(x):
    hi = x.astype(jnp.bfloat16)
    lo = (x - hi.astype(jnp.float32)).astype(jnp.bfloat16)
    return hi, lo

def _dot_nt(a, b):
    return lax.dot_general(a, b, (((1,), (1,)), ((), ())), preferred_element_type=jnp.float32)

def _dot3(a, b):
    return _dot_nt(a[0], b[0]) + _dot_nt(a[0], b[1]) + _dot_nt(a[1], b[0])

def _dot_nn(a, b):
    return lax.dot_general(a, b, (((1,), (0,)), ((), ())), preferred_element_type=jnp.float32)


def _proj_kernel(et_hi_ref, et_lo_ref, v_ref, outer_ref, inner_ref, gram_ref):
    @pl.when(pl.program_id(0) == 0)
    def _():
        outer_ref[...] = jnp.zeros_like(outer_ref)
        inner_ref[...] = jnp.zeros_like(inner_ref)
        gram_ref[...] = jnp.zeros_like(gram_ref)
    et = (et_hi_ref[...], et_lo_ref[...])
    outer = _split(v_ref[0])
    inner = _split(v_ref[1])
    outer_ref[...] += _dot_nn(outer[0], et[0]) + _dot_nn(outer[0], et[1]) + _dot_nn(outer[1], et[0])
    inner_ref[...] += _dot_nn(inner[0], et[0]) + _dot_nn(inner[0], et[1]) + _dot_nn(inner[1], et[0])
    gram_ref[...] += _dot3(inner, outer)


def project(eigvecs, panel_t, tile):
    n, m = eigvecs.shape
    k = panel_t.shape[1]
    high = lax.reduce_precision(eigvecs, exponent_bits=8, mantissa_bits=7)
    et_hi = high.T.astype(jnp.bfloat16)
    et_lo = (eigvecs - high).T.astype(jnp.bfloat16)
    return pl.pallas_call(
        _proj_kernel,
        grid=(m // tile,),
        in_specs=[pl.BlockSpec((tile, n), lambda i: (i, 0)),
                  pl.BlockSpec((tile, n), lambda i: (i, 0)),
                  pl.BlockSpec((2, k, tile), lambda i: (0, 0, i))],
        out_specs=[pl.BlockSpec((k, n), lambda i: (0, 0)),
                   pl.BlockSpec((k, n), lambda i: (0, 0)),
                   pl.BlockSpec((k, k), lambda i: (0, 0))],
        out_shape=[jax.ShapeDtypeStruct((k, n), jnp.float32),
                   jax.ShapeDtypeStruct((k, n), jnp.float32),
                   jax.ShapeDtypeStruct((k, k), jnp.float32)],
        compiler_params=pltpu.CompilerParams(dimension_semantics=("arbitrary",)),
    )(et_hi, et_lo, panel_t)


def body(eigvecs, basis, coupling):
    panel = lax.all_gather(jnp.swapaxes(basis, 1, 2), "col", axis=1, tiled=True)
    n = eigvecs.shape[0]
    k = panel.shape[1]
    rows = lax.axis_size("row")
    outer_t, inner_t, gram = butterfly_sum(project(eigvecs, panel, 2048), "row", rows)
    proj_inner = inner_t.T
    proj_outer = outer_t.T
    reflected_inner = large_product(proj_inner, coupling[1], ((1,), (1,)))
    proj_outer = proj_outer - large_product(reflected_inner, gram, ((1,), (0,)))
    reflected_outer = large_product(proj_outer, coupling[0], ((1,), (1,)))
    reflected = jnp.stack([reflected_outer, reflected_inner], axis=1)
    current = eigvecs - large_product(reflected, panel, ((1, 2), (0, 1)))
    return lax.all_to_all(current, "row", split_axis=0, concat_axis=1, tiled=True)


def solution(mesh):
    placed = (P("col", "row"), P(None, "row", "col"), P())
    return jax.shard_map(
        body, mesh=mesh, in_specs=placed, out_specs=P(("col", "row"), None), check_vma=False
    )
```
